32 devices in a mesh: row: 8 (over y, x, core), col: 4 (over z).
Axes of the slice: x: 2, y: 2, z: 4, core: 2. Of those that a mesh axis runs over, the one named last changes fastest.
Arguments:
- adjacency: float32 [1024, 32768], P('row', 'col'), may hold values from 0 to 0.99, as said below
Outputs:
- tom: float32 [1024, 1024], P('row', 'col')
The draws below stay inside these ranges and needn't reach their ends.
Inputs may be any that keep to these rules, and one draw needn't show every extreme that they name: `adjacency`: every entry is nonnegative and below 0.99.
All inputs are finite; a program needn't handle non-finite values.
Results may differ from the reference program's by a relative error of at most 0.000059.
Values sent between devices are 32-bit elements; how exact they have to be, the bound alone decides.
No kernel may reach another device: no remote copies, remote signals or barrier semaphores. Data moves between devices by JAX's collectives and lax.ppermute only.
A program may use at most 64 MiB of HBM per device.

```python
import math
import jax
import jax.numpy as jnp
from jax import lax

PROBES = 32768
ROWS = 1024
WINDOW = 256
SLAB = 8192
N_COL = 4


def draw_adjacency(key, part):
    key_module, key_rows, key_cols, key_vals, key_pairs = jax.random.split(key, 5)
    modules = max(PROBES // 512, 4)
    probe_module = jax.random.randint(key_module, (PROBES,), 0, modules, dtype=jnp.int32)
    window_index = jnp.arange(ROWS, dtype=jnp.int32)
    probe_index = (window_index // WINDOW * SLAB + window_index % WINDOW).astype(jnp.int32)
    row_module = jnp.take(probe_module, probe_index, axis=0)
    uniform_part = jax.random.uniform(key_vals, (ROWS, PROBES), jnp.float32, 0.0, 1.0)
    lowest_row = math.log(0.002)
    lowest_col = math.log(0.1)
    lowest_pair = math.log(0.003)
    highest_pair = math.log(0.3)
    values = uniform_part * uniform_part
    pair_strength = jnp.exp(jax.random.uniform(key_pairs, (modules, modules), jnp.float32, lowest_pair, highest_pair))
    module_ids = jnp.arange(modules, dtype=jnp.int32)
    pair_strength = jnp.where(module_ids[:, None] == module_ids[None, :], jnp.float32(1.0), pair_strength)
    row_table = jnp.take(pair_strength, row_module, axis=0)
    factor = jnp.take(row_table, probe_module, axis=1)
    row_strength = jnp.exp(jax.random.uniform(key_rows, (ROWS, 1), jnp.float32, lowest_row, 0.0))
    col_strength = jnp.exp(jax.random.uniform(key_cols, (1, PROBES), jnp.float32, lowest_col, 0.0))
    return 0.99 * row_strength * col_strength * factor * values


def setup_inputs(seed: int = 0) -> dict:
    key_of = jax.random.split(jax.random.key(seed), 2)
    return {
        "adjacency": draw_adjacency(jax.random.fold_in(key_of[1], 71), 0),
    }


def reference(adjacency):
    shared = lax.dot_general(adjacency, adjacency, (((1,), (1,)), ((), ())), precision=lax.Precision.HIGHEST, preferred_element_type=jnp.float32)
    degree = jnp.sum(adjacency, axis=1)
    window = ROWS // N_COL
    slab_width = PROBES // N_COL
    window_index = jnp.arange(ROWS, dtype=jnp.int32)
    probe_index = ((window_index // window) * slab_width + window_index % window).astype(jnp.int32)
    linked = jnp.take(adjacency, probe_index, axis=1)
    smaller = jnp.minimum(degree[:, None], degree[None, :])
    return (shared + linked) / (smaller + 1.0 - linked)
```

```python
import jax
import jax.numpy as jnp
from jax import lax
from jax.sharding import PartitionSpec as P


def inner_rows(left, right):
    return lax.dot_general(
        left,
        right,
        (((1,), (1,)), ((), ())),
        precision=lax.Precision.HIGHEST,
        preferred_element_type=jnp.float32,
    )


def finish(shared_sum, linked, own_degree, col_degree):
    smaller = jnp.minimum(own_degree[:, None], col_degree[None, :])
    return (shared_sum + linked) / (smaller + 1.0 - linked)


def degrees(adjacency, window):
    n_row = lax.axis_size("row")
    n_col = lax.axis_size("col")
    strip_rows = adjacency.shape[0]
    row_sum = jnp.sum(adjacency, axis=1)
    every = lax.all_gather(row_sum, ("row", "col"), axis=0, tiled=True)
    every = every.reshape(n_row, n_col, strip_rows).sum(axis=1).reshape(-1)
    own = lax.dynamic_slice_in_dim(every, lax.axis_index("row") * strip_rows, strip_rows, 0)
    col = lax.dynamic_slice_in_dim(every, lax.axis_index("col") * window, window, 0)
    return own, col


def solution(mesh):
    placed = (P("row", "col"),)
    return jax.shard_map(
        body, mesh=mesh, in_specs=placed, out_specs=P("row", "col"), check_vma=False
    )


def body(adjacency):
    strip_rows = adjacency.shape[0]
    window = strip_rows * lax.axis_size("row") // lax.axis_size("col")
    pieces = lax.all_to_all(adjacency, "row", split_axis=1, concat_axis=0, tiled=True)
    part = lax.psum_scatter(inner_rows(pieces, pieces), "row", scatter_dimension=0, tiled=True)
    shared_sum = lax.psum_scatter(part, "col", scatter_dimension=1, tiled=True)
    own_degree = lax.psum(jnp.sum(adjacency, axis=1), "col")
    all_degree = lax.all_gather(own_degree, "row", axis=0, tiled=True)
    col_degree = lax.dynamic_slice_in_dim(all_degree, lax.axis_index("col") * window, window, 0)
    linked = adjacency[:, :window]
    return finish(shared_sum, linked, own_degree, col_degree)
```

```python
import jax
import jax.numpy as jnp
from jax import lax
from jax.sharding import PartitionSpec as P


def inner_rows(left, right):
    return lax.dot_general(
        left,
        right,
        (((1,), (1,)), ((), ())),
        precision=lax.Precision.HIGH,
        preferred_element_type=jnp.float32,
    )


def finish(shared_sum, linked, own_degree, col_degree):
    smaller = jnp.minimum(own_degree[:, None], col_degree[None, :])
    return (shared_sum + linked) / (smaller + 1.0 - linked)


def degrees(adjacency, window):
    n_row = lax.axis_size("row")
    n_col = lax.axis_size("col")
    strip_rows = adjacency.shape[0]
    row_sum = jnp.sum(adjacency, axis=1)
    every = lax.all_gather(row_sum, ("row", "col"), axis=0, tiled=True)
    every = every.reshape(n_row, n_col, strip_rows).sum(axis=1).reshape(-1)
    own = lax.dynamic_slice_in_dim(every, lax.axis_index("row") * strip_rows, strip_rows, 0)
    col = lax.dynamic_slice_in_dim(every, lax.axis_index("col") * window, window, 0)
    return own, col


def solution(mesh):
    placed = (P("row", "col"),)
    return jax.shard_map(
        body, mesh=mesh, in_specs=placed, out_specs=P("row", "col"), check_vma=False
    )


def col_reduce_scatter(part):
    n_col = lax.axis_size("col")
    me = lax.axis_index("col")
    rows, cols = part.shape
    width = cols // n_col
    blocks = part.reshape(rows, n_col, width)
    total = lax.dynamic_index_in_dim(blocks, me, 1, keepdims=False)
    for s in range(1, n_col):
        send = lax.dynamic_index_in_dim(blocks, (me + s) % n_col, 1, keepdims=False)
        perm = [(i, (i + s) % n_col) for i in range(n_col)]
        total = total + lax.ppermute(send, "col", perm)
    return total


def body(adjacency):
    strip_rows = adjacency.shape[0]
    window = strip_rows * lax.axis_size("row") // lax.axis_size("col")
    pieces = lax.all_to_all(adjacency, "row", split_axis=1, concat_axis=0, tiled=True)
    part = lax.psum_scatter(inner_rows(pieces, pieces), "row", scatter_dimension=0, tiled=True)
    own_degree = lax.psum(jnp.sum(adjacency, axis=1), "col")
    all_degree = lax.all_gather(own_degree, "row", axis=0, tiled=True)
    col_degree = lax.dynamic_slice_in_dim(all_degree, lax.axis_index("col") * window, window, 0)
    part, own_degree, col_degree = lax.optimization_barrier((part, own_degree, col_degree))
    shared_sum = col_reduce_scatter(part)
    linked = adjacency[:, :window]
    return finish(shared_sum, linked, own_degree, col_degree)
```

```python
import jax
import jax.numpy as jnp
from jax import lax
from jax.sharding import PartitionSpec as P


def inner_rows(left, right):
    return lax.dot_general(
        left,
        right,
        (((1,), (1,)), ((), ())),
        precision=lax.Precision.HIGH,
        preferred_element_type=jnp.float32,
    )


def finish(shared_sum, linked, own_degree, col_degree):
    smaller = jnp.minimum(own_degree[:, None], col_degree[None, :])
    return (shared_sum + linked) / (smaller + 1.0 - linked)


def degrees(adjacency, window):
    n_row = lax.axis_size("row")
    n_col = lax.axis_size("col")
    strip_rows = adjacency.shape[0]
    row_sum = jnp.sum(adjacency, axis=1)
    every = lax.all_gather(row_sum, ("row", "col"), axis=0, tiled=True)
    every = every.reshape(n_row, n_col, strip_rows).sum(axis=1).reshape(-1)
    own = lax.dynamic_slice_in_dim(every, lax.axis_index("row") * strip_rows, strip_rows, 0)
    col = lax.dynamic_slice_in_dim(every, lax.axis_index("col") * window, window, 0)
    return own, col


def solution(mesh):
    placed = (P("row", "col"),)
    return jax.shard_map(
        body, mesh=mesh, in_specs=placed, out_specs=P("row", "col"), check_vma=False
    )


def col_reduce_scatter(part):
    n_col = lax.axis_size("col")
    me = lax.axis_index("col")
    rows, cols = part.shape
    width = cols // n_col
    blocks = part.reshape(rows, n_col, width)
    total = lax.dynamic_index_in_dim(blocks, me, 1, keepdims=False)
    for s in range(1, n_col):
        send = lax.dynamic_index_in_dim(blocks, (me + s) % n_col, 1, keepdims=False)
        perm = [(i, (i + s) % n_col) for i in range(n_col)]
        total = total + lax.ppermute(send, "col", perm)
    return total
from jax.experimental.layout import Layout, with_layout_constraint


def body(adjacency):
    strip_rows, cols = adjacency.shape
    n_row = lax.axis_size("row")
    window = strip_rows * n_row // lax.axis_size("col")
    piece = cols // n_row
    chunks = jnp.stack([adjacency[:, d * piece : (d + 1) * piece] for d in range(n_row)])
    chunks = with_layout_constraint(chunks, Layout((0, 1, 2)))
    pieces = lax.all_to_all(chunks, "row", split_axis=0, concat_axis=0, tiled=True)
    pieces = with_layout_constraint(pieces, Layout((0, 1, 2)))
    pieces = pieces.reshape(n_row * strip_rows, cols // n_row)
    part = lax.psum_scatter(inner_rows(pieces, pieces), "row", scatter_dimension=0, tiled=True)
    own_degree = lax.psum(jnp.sum(adjacency, axis=1), "col")
    all_degree = lax.all_gather(own_degree, "row", axis=0, tiled=True)
    col_degree = lax.dynamic_slice_in_dim(all_degree, lax.axis_index("col") * window, window, 0)
    part, own_degree, col_degree = lax.optimization_barrier((part, own_degree, col_degree))
    shared_sum = col_reduce_scatter(part)
    linked = adjacency[:, :window]
    return finish(shared_sum, linked, own_degree, col_degree)
```

```python
import jax
import jax.numpy as jnp
from jax import lax
from jax.sharding import Mesh
from jax.sharding import PartitionSpec as P
from jax.experimental.layout import Layout, with_layout_constraint

ROW = ("chip", "core")


def inner_rows(left, right):
    return lax.dot_general(
        left,
        right,
        (((1,), (1,)), ((), ())),
        precision=lax.Precision.HIGH,
        preferred_element_type=jnp.float32,
    )


def col_reduce_scatter(part):
    n_col = lax.axis_size("col")
    me = lax.axis_index("col")
    rows, cols = part.shape
    width = cols // n_col
    blocks = part.reshape(rows, n_col, width)
    total = lax.dynamic_index_in_dim(blocks, me, 1, keepdims=False)
    for s in range(1, n_col):
        send = lax.dynamic_index_in_dim(blocks, (me + s) % n_col, 1, keepdims=False)
        perm = [(i, (i + s) % n_col) for i in range(n_col)]
        total = total + lax.ppermute(send, "col", perm)
    return total


def row_reduce_scatter(pieces):
    n_chip = lax.axis_size("chip")
    n_core = lax.axis_size("core")
    me = lax.axis_index("core")
    rows, depth = pieces.shape
    strip = rows // (n_chip * n_core)
    paired = inner_rows(pieces, pieces).reshape(n_chip, n_core, strip, rows)
    on_chip = lax.dynamic_index_in_dim(paired, me, 1, keepdims=False)
    for s in range(1, n_core):
        send = lax.dynamic_index_in_dim(paired, (me + s) % n_core, 1, keepdims=False)
        perm = [(i, (i + s) % n_core) for i in range(n_core)]
        on_chip = on_chip + lax.ppermute(send, "core", perm)
    blocks = on_chip.reshape(n_chip, strip, rows)
    mine = lax.axis_index("chip")
    total = lax.dynamic_index_in_dim(blocks, mine, 0, keepdims=False)
    for s in range(1, n_chip):
        send = lax.dynamic_index_in_dim(blocks, (mine + s) % n_chip, 0, keepdims=False)
        perm = [(i, (i + s) % n_chip) for i in range(n_chip)]
        total = total + lax.ppermute(send, "chip", perm)
    return total


def body(adjacency):
    strip_rows, cols = adjacency.shape
    n_row = lax.axis_size(ROW)
    window = strip_rows * n_row // lax.axis_size("col")
    piece = cols // n_row
    chunks = jnp.stack([adjacency[:, d * piece : (d + 1) * piece] for d in range(n_row)])
    chunks = with_layout_constraint(chunks, Layout((0, 1, 2)))
    pieces = lax.all_to_all(chunks, ROW, split_axis=0, concat_axis=0, tiled=True)
    pieces = with_layout_constraint(pieces, Layout((0, 1, 2)))
    own_degree = lax.psum(jnp.sum(adjacency, axis=1), "col")
    all_degree = lax.all_gather(own_degree, ROW, axis=0, tiled=True)
    col_degree = lax.dynamic_slice_in_dim(all_degree, lax.axis_index("col") * window, window, 0)
    pieces, own_degree, col_degree = lax.optimization_barrier((pieces, own_degree, col_degree))
    pieces = pieces.reshape(n_row * strip_rows, piece)
    shared_sum = col_reduce_scatter(row_reduce_scatter(pieces))
    linked = adjacency[:, :window]
    smaller = jnp.minimum(own_degree[:, None], col_degree[None, :])
    return (shared_sum + linked) / (smaller + 1.0 - linked)


def solution(mesh):
    n_row, n_col = mesh.devices.shape
    split = Mesh(mesh.devices.reshape(n_row // 2, 2, n_col), ("chip", "core", "col"))
    placed = (P(ROW, "col"),)
    return jax.shard_map(body, mesh=split, in_specs=placed, out_specs=P(ROW, "col"), check_vma=False)
```

```python
import jax
import jax.numpy as jnp
from jax import lax
from jax.sharding import Mesh
from jax.sharding import PartitionSpec as P
from jax.experimental import pallas as pl
from jax.experimental.layout import Layout, with_layout_constraint

ROW = ("chip", "core")


def inner_rows(left, right):
    return lax.dot_general(
        left,
        right,
        (((1,), (1,)), ((), ())),
        precision=lax.Precision.HIGH,
        preferred_element_type=jnp.float32,
    )


def _copy_block(block_ref, out_ref):
    out_ref[0] = block_ref[...]


def column_chunks(adjacency, n_chunks):
    rows, cols = adjacency.shape
    piece = cols // n_chunks
    return pl.pallas_call(
        _copy_block,
        grid=(n_chunks,),
        in_specs=[pl.BlockSpec((rows, piece), lambda d: (0, d))],
        out_specs=pl.BlockSpec((1, rows, piece), lambda d: (d, 0, 0)),
        out_shape=jax.ShapeDtypeStruct((n_chunks, rows, piece), adjacency.dtype),
    )(adjacency)


def col_reduce_scatter(part):
    n_col = lax.axis_size("col")
    me = lax.axis_index("col")
    rows, cols = part.shape
    width = cols // n_col
    blocks = part.reshape(rows, n_col, width)
    total = lax.dynamic_index_in_dim(blocks, me, 1, keepdims=False)
    for s in range(1, n_col):
        send = lax.dynamic_index_in_dim(blocks, (me + s) % n_col, 1, keepdims=False)
        perm = [(i, (i + s) % n_col) for i in range(n_col)]
        total = total + lax.ppermute(send, "col", perm)
    return total


def row_reduce_scatter(pieces):
    n_chip = lax.axis_size("chip")
    n_core = lax.axis_size("core")
    me = lax.axis_index("core")
    rows, depth = pieces.shape
    strip = rows // (n_chip * n_core)
    paired = inner_rows(pieces, pieces).reshape(n_chip, n_core, strip, rows)
    on_chip = lax.dynamic_index_in_dim(paired, me, 1, keepdims=False)
    for s in range(1, n_core):
        send = lax.dynamic_index_in_dim(paired, (me + s) % n_core, 1, keepdims=False)
        perm = [(i, (i + s) % n_core) for i in range(n_core)]
        on_chip = on_chip + lax.ppermute(send, "core", perm)
    blocks = on_chip.reshape(n_chip, strip, rows)
    mine = lax.axis_index("chip")
    total = lax.dynamic_index_in_dim(blocks, mine, 0, keepdims=False)
    for s in range(1, n_chip):
        send = lax.dynamic_index_in_dim(blocks, (mine + s) % n_chip, 0, keepdims=False)
        perm = [(i, (i + s) % n_chip) for i in range(n_chip)]
        total = total + lax.ppermute(send, "chip", perm)
    return total


def body(adjacency):
    strip_rows, cols = adjacency.shape
    n_row = lax.axis_size(ROW)
    window = strip_rows * n_row // lax.axis_size("col")
    piece = cols // n_row
    chunks = column_chunks(adjacency, n_row)
    pieces = lax.all_to_all(chunks, ROW, split_axis=0, concat_axis=0, tiled=True)
    pieces = with_layout_constraint(pieces, Layout((0, 1, 2)))
    own_degree = lax.psum(jnp.sum(adjacency, axis=1), "col")
    all_degree = lax.all_gather(own_degree, ROW, axis=0, tiled=True)
    col_degree = lax.dynamic_slice_in_dim(all_degree, lax.axis_index("col") * window, window, 0)
    pieces, own_degree, col_degree = lax.optimization_barrier((pieces, own_degree, col_degree))
    pieces = pieces.reshape(n_row * strip_rows, piece)
    shared_sum = col_reduce_scatter(row_reduce_scatter(pieces))
    linked = adjacency[:, :window]
    smaller = jnp.minimum(own_degree[:, None], col_degree[None, :])
    return (shared_sum + linked) / (smaller + 1.0 - linked)


def solution(mesh):
    n_row, n_col = mesh.devices.shape
    split = Mesh(mesh.devices.reshape(n_row // 2, 2, n_col), ("chip", "core", "col"))
    placed = (P(ROW, "col"),)
    return jax.shard_map(body, mesh=split, in_specs=placed, out_specs=P(ROW, "col"), check_vma=False)
```

```python
import jax
import jax.numpy as jnp
from jax import lax
from jax.sharding import Mesh
from jax.sharding import PartitionSpec as P
from jax.experimental import pallas as pl
from jax.experimental.layout import Layout, with_layout_constraint

ROW = ("chip", "core")


def inner_rows(left, right):
    return lax.dot_general(
        left,
        right,
        (((1,), (1,)), ((), ())),
        precision=lax.Precision.HIGH,
        preferred_element_type=jnp.float32,
    )


def _copy_block(block_ref, out_ref):
    out_ref[0] = block_ref[...]


def column_chunks(adjacency, n_chunks):
    rows, cols = adjacency.shape
    piece = cols // n_chunks
    return pl.pallas_call(
        _copy_block,
        grid=(n_chunks,),
        in_specs=[pl.BlockSpec((rows, piece), lambda d: (0, d))],
        out_specs=pl.BlockSpec((1, rows, piece), lambda d: (d, 0, 0)),
        out_shape=jax.ShapeDtypeStruct((n_chunks, rows, piece), adjacency.dtype),
    )(adjacency)


def col_reduce_scatter(part):
    n_col = lax.axis_size("col")
    me = lax.axis_index("col")
    rows, cols = part.shape
    width = cols // n_col
    blocks = part.reshape(rows, n_col, width)
    total = lax.dynamic_index_in_dim(blocks, me, 1, keepdims=False)
    for s in range(1, n_col):
        send = lax.dynamic_index_in_dim(blocks, (me + s) % n_col, 1, keepdims=False)
        perm = [(i, (i + s) % n_col) for i in range(n_col)]
        total = total + lax.ppermute(send, "col", perm)
    return total


def row_reduce_scatter(pieces, right):
    n_chip = lax.axis_size("chip")
    n_core = lax.axis_size("core")
    me = lax.axis_index("core")
    rows = pieces.shape[0]
    width = right.shape[0]
    strip = rows // (n_chip * n_core)
    paired = inner_rows(pieces, right).reshape(n_chip, n_core, strip, width)
    on_chip = lax.dynamic_index_in_dim(paired, me, 1, keepdims=False)
    for s in range(1, n_core):
        send = lax.dynamic_index_in_dim(paired, (me + s) % n_core, 1, keepdims=False)
        perm = [(i, (i + s) % n_core) for i in range(n_core)]
        on_chip = on_chip + lax.ppermute(send, "core", perm)
    blocks = on_chip
    mine = lax.axis_index("chip")
    total = lax.dynamic_index_in_dim(blocks, mine, 0, keepdims=False)
    for s in range(1, n_chip):
        send = lax.dynamic_index_in_dim(blocks, (mine + s) % n_chip, 0, keepdims=False)
        perm = [(i, (i + s) % n_chip) for i in range(n_chip)]
        total = total + lax.ppermute(send, "chip", perm)
    return total


def body(adjacency):
    strip_rows, cols = adjacency.shape
    n_row = lax.axis_size(ROW)
    n_col = lax.axis_size("col")
    window = strip_rows * n_row // n_col
    piece = cols // n_row
    chunks = column_chunks(adjacency, n_row)
    pieces = lax.all_to_all(chunks, ROW, split_axis=0, concat_axis=0, tiled=True)
    pieces = with_layout_constraint(pieces, Layout((0, 1, 2)))
    own_degree = lax.psum(jnp.sum(adjacency, axis=1), "col")
    all_degree = lax.all_gather(own_degree, ROW, axis=0, tiled=True)
    col_degree = lax.dynamic_slice_in_dim(all_degree, lax.axis_index("col") * window, window, 0)
    pieces, own_degree, col_degree = lax.optimization_barrier((pieces, own_degree, col_degree))
    pieces = pieces.reshape(n_row * strip_rows, piece)
    groups = 2 if window % 256 == 0 else 1
    sub = window // groups
    by_group = pieces.reshape(n_col, groups, sub, piece)
    outs = []
    for g in range(groups):
        right = by_group[:, g].reshape(n_col * sub, piece)
        outs.append(col_reduce_scatter(row_reduce_scatter(pieces, right)))
    shared_sum = jnp.stack(outs, axis=1).reshape(strip_rows, window)
    linked = adjacency[:, :window]
    smaller = jnp.minimum(own_degree[:, None], col_degree[None, :])
    return (shared_sum + linked) / (smaller + 1.0 - linked)


def solution(mesh):
    n_row, n_col = mesh.devices.shape
    split = Mesh(mesh.devices.reshape(n_row // 2, 2, n_col), ("chip", "core", "col"))
    placed = (P(ROW, "col"),)
    return jax.shard_map(body, mesh=split, in_specs=placed, out_specs=P(ROW, "col"), check_vma=False)
```

```python
import jax
import jax.numpy as jnp
from jax import lax
from jax.sharding import Mesh
from jax.sharding import PartitionSpec as P
from jax.experimental import pallas as pl
from jax.experimental.layout import Layout, with_layout_constraint

ROW = ("chip", "core")


def inner_rows(left, right):
    return lax.dot_general(
        left,
        right,
        (((1,), (1,)), ((), ())),
        precision=lax.Precision.HIGH,
        preferred_element_type=jnp.float32,
    )


def _copy_blocks(block_ref, out_ref):
    per_step, _, width = out_ref.shape
    for t in range(per_step):
        out_ref[t] = block_ref[:, t * width : (t + 1) * width]


def column_chunks(adjacency, n_chunks):
    rows, cols = adjacency.shape
    piece = cols // n_chunks
    per_step = 4 if n_chunks % 4 == 0 else 1
    return pl.pallas_call(
        _copy_blocks,
        grid=(n_chunks // per_step,),
        in_specs=[pl.BlockSpec((rows, piece * per_step), lambda d: (0, d))],
        out_specs=pl.BlockSpec((per_step, rows, piece), lambda d: (d, 0, 0)),
        out_shape=jax.ShapeDtypeStruct((n_chunks, rows, piece), adjacency.dtype),
    )(adjacency)


def col_reduce_scatter(part):
    n_col = lax.axis_size("col")
    me = lax.axis_index("col")
    rows, cols = part.shape
    width = cols // n_col
    blocks = part.reshape(rows, n_col, width)
    total = lax.dynamic_index_in_dim(blocks, me, 1, keepdims=False)
    for s in range(1, n_col):
        send = lax.dynamic_index_in_dim(blocks, (me + s) % n_col, 1, keepdims=False)
        perm = [(i, (i + s) % n_col) for i in range(n_col)]
        total = total + lax.ppermute(send, "col", perm)
    return total


def row_reduce_scatter(pieces, right):
    n_chip = lax.axis_size("chip")
    n_core = lax.axis_size("core")
    me = lax.axis_index("core")
    rows = pieces.shape[0]
    width = right.shape[0]
    strip = rows // (n_chip * n_core)
    paired = inner_rows(pieces, right).reshape(n_chip, n_core, strip, width)
    on_chip = lax.dynamic_index_in_dim(paired, me, 1, keepdims=False)
    for s in range(1, n_core):
        send = lax.dynamic_index_in_dim(paired, (me + s) % n_core, 1, keepdims=False)
        perm = [(i, (i + s) % n_core) for i in range(n_core)]
        on_chip = on_chip + lax.ppermute(send, "core", perm)
    blocks = on_chip
    mine = lax.axis_index("chip")
    total = lax.dynamic_index_in_dim(blocks, mine, 0, keepdims=False)
    for s in range(1, n_chip):
        send = lax.dynamic_index_in_dim(blocks, (mine + s) % n_chip, 0, keepdims=False)
        perm = [(i, (i + s) % n_chip) for i in range(n_chip)]
        total = total + lax.ppermute(send, "chip", perm)
    return total


def body(adjacency):
    strip_rows, cols = adjacency.shape
    n_row = lax.axis_size(ROW)
    n_col = lax.axis_size("col")
    window = strip_rows * n_row // n_col
    piece = cols // n_row
    chunks = column_chunks(adjacency, n_row)
    pieces = lax.all_to_all(chunks, ROW, split_axis=0, concat_axis=0, tiled=True)
    pieces = with_layout_constraint(pieces, Layout((0, 1, 2)))
    own_degree = lax.psum(jnp.sum(adjacency, axis=1), "col")
    all_degree = lax.all_gather(own_degree, ROW, axis=0, tiled=True)
    col_degree = lax.dynamic_slice_in_dim(all_degree, lax.axis_index("col") * window, window, 0)
    pieces, own_degree, col_degree = lax.optimization_barrier((pieces, own_degree, col_degree))
    pieces = pieces.reshape(n_row * strip_rows, piece)
    groups = 2 if window % 256 == 0 else 1
    sub = window // groups
    by_group = pieces.reshape(n_col, groups, sub, piece)
    outs = []
    for g in range(groups):
        right = by_group[:, g].reshape(n_col * sub, piece)
        outs.append(col_reduce_scatter(row_reduce_scatter(pieces, right)))
    shared_sum = jnp.stack(outs, axis=1).reshape(strip_rows, window)
    linked = adjacency[:, :window]
    smaller = jnp.minimum(own_degree[:, None], col_degree[None, :])
    return (shared_sum + linked) / (smaller + 1.0 - linked)


def solution(mesh):
    n_row, n_col = mesh.devices.shape
    split = Mesh(mesh.devices.reshape(n_row // 2, 2, n_col), ("chip", "core", "col"))
    placed = (P(ROW, "col"),)
    return jax.shard_map(body, mesh=split, in_specs=placed, out_specs=P(ROW, "col"), check_vma=False)
```

```python
import jax
import jax.numpy as jnp
from jax import lax
from jax.sharding import Mesh
from jax.sharding import PartitionSpec as P
from jax.experimental import pallas as pl
from jax.experimental.layout import Layout, with_layout_constraint

ROW = ("chip", "core")


def inner_rows(left, right):
    return lax.dot_general(
        left,
        right,
        (((1,), (1,)), ((), ())),
        precision=lax.Precision.HIGH,
        preferred_element_type=jnp.float32,
    )


def _copy_blocks(block_ref, out_ref):
    per_step, _, width = out_ref.shape
    for t in range(per_step):
        out_ref[t] = block_ref[:, t * width : (t + 1) * width]


def column_chunks(adjacency, n_chunks):
    rows, cols = adjacency.shape
    piece = cols // n_chunks
    per_step = 4 if n_chunks % 4 == 0 else 1
    return pl.pallas_call(
        _copy_blocks,
        grid=(n_chunks // per_step,),
        in_specs=[pl.BlockSpec((rows, piece * per_step), lambda d: (0, d))],
        out_specs=pl.BlockSpec((per_step, rows, piece), lambda d: (d, 0, 0)),
        out_shape=jax.ShapeDtypeStruct((n_chunks, rows, piece), adjacency.dtype),
    )(adjacency)


def col_reduce_scatter(part):
    n_col = lax.axis_size("col")
    me = lax.axis_index("col")
    rows, cols = part.shape
    width = cols // n_col
    blocks = part.reshape(rows, n_col, width)
    total = lax.dynamic_index_in_dim(blocks, me, 1, keepdims=False)
    for s in range(1, n_col):
        send = lax.dynamic_index_in_dim(blocks, (me + s) % n_col, 1, keepdims=False)
        perm = [(i, (i + s) % n_col) for i in range(n_col)]
        total = total + lax.ppermute(send, "col", perm)
    return total


def row_reduce_scatter(gram, core_major):
    n_chip = lax.axis_size("chip")
    n_core = lax.axis_size("core")
    me = lax.axis_index("core")
    rows, width = gram.shape
    strip = rows // (n_chip * n_core)
    if core_major:
        paired, axis = gram.reshape(n_core, n_chip, strip, width), 0
    else:
        paired, axis = gram.reshape(n_chip, n_core, strip, width), 1
    on_chip = lax.dynamic_index_in_dim(paired, me, axis, keepdims=False)
    for s in range(1, n_core):
        send = lax.dynamic_index_in_dim(paired, (me + s) % n_core, axis, keepdims=False)
        perm = [(i, (i + s) % n_core) for i in range(n_core)]
        on_chip = on_chip + lax.ppermute(send, "core", perm)
    blocks = on_chip
    mine = lax.axis_index("chip")
    total = lax.dynamic_index_in_dim(blocks, mine, 0, keepdims=False)
    for s in range(1, n_chip):
        if n_chip & (n_chip - 1) == 0:
            peer, perm = mine ^ s, [(i, i ^ s) for i in range(n_chip)]
        else:
            peer, perm = (mine + s) % n_chip, [(i, (i + s) % n_chip) for i in range(n_chip)]
        send = lax.dynamic_index_in_dim(blocks, peer, 0, keepdims=False)
        total = total + lax.ppermute(send, "chip", perm)
    return total


def chip_reduce_scatter(on_chip):
    n_chip = lax.axis_size("chip")
    rows, width = on_chip.shape
    blocks = on_chip.reshape(n_chip, rows // n_chip, width)
    mine = lax.axis_index("chip")
    total = lax.dynamic_index_in_dim(blocks, mine, 0, keepdims=False)
    for s in range(1, n_chip):
        if n_chip & (n_chip - 1) == 0:
            peer, perm = mine ^ s, [(i, i ^ s) for i in range(n_chip)]
        else:
            peer, perm = (mine + s) % n_chip, [(i, (i + s) % n_chip) for i in range(n_chip)]
        send = lax.dynamic_index_in_dim(blocks, peer, 0, keepdims=False)
        total = total + lax.ppermute(send, "chip", perm)
    return total


def body(adjacency):
    strip_rows, cols = adjacency.shape
    n_row = lax.axis_size(ROW)
    n_col = lax.axis_size("col")
    n_core = lax.axis_size("core")
    window = strip_rows * n_row // n_col
    piece = cols // n_row
    core_major = n_col == lax.axis_size("chip") and window == n_core * strip_rows
    chunks = column_chunks(adjacency, n_row)
    order = ("core", "chip") if core_major else ROW
    pieces = lax.all_to_all(chunks, order, split_axis=0, concat_axis=0, tiled=True)
    pieces = with_layout_constraint(pieces, Layout((0, 1, 2)))
    own_degree = lax.psum(jnp.sum(adjacency, axis=1), "col")
    all_degree = lax.all_gather(own_degree, ROW, axis=0, tiled=True)
    col_degree = lax.dynamic_slice_in_dim(all_degree, lax.axis_index("col") * window, window, 0)
    pieces, own_degree, col_degree = lax.optimization_barrier((pieces, own_degree, col_degree))
    outs = []
    if core_major:
        groups = n_core
        flat = pieces.reshape(n_row * strip_rows, piece)
        by_core = pieces.reshape(n_core, n_col * strip_rows, piece)
        me = lax.axis_index("core")
        for g in range(groups):
            right = by_core[g]
            on_chip = None
            for s in range(1, n_core):
                left = lax.dynamic_index_in_dim(by_core, (me + s) % n_core, 0, keepdims=False)
                perm = [(i, (i + s) % n_core) for i in range(n_core)]
                got = lax.ppermute(inner_rows(left, right), "core", perm)
                on_chip = got if on_chip is None else on_chip + got
            left = lax.dynamic_index_in_dim(by_core, me, 0, keepdims=False)
            on_chip = inner_rows(left, right) + on_chip
            outs.append(col_reduce_scatter(chip_reduce_scatter(on_chip)))
    else:
        groups = 2 if window % 256 == 0 else 1
        sub = window // groups
        flat = pieces.reshape(n_row * strip_rows, piece)
        by_group = flat.reshape(n_col, groups, sub, piece)
        for g in range(groups):
            right = by_group[:, g].reshape(n_col * sub, piece)
            outs.append(col_reduce_scatter(row_reduce_scatter(inner_rows(flat, right), False)))
    shared_sum = jnp.stack(outs, axis=1).reshape(strip_rows, window)
    linked = adjacency[:, :window]
    smaller = jnp.minimum(own_degree[:, None], col_degree[None, :])
    return (shared_sum + linked) / (smaller + 1.0 - linked)


def solution(mesh):
    n_row, n_col = mesh.devices.shape
    split = Mesh(mesh.devices.reshape(n_row // 2, 2, n_col), ("chip", "core", "col"))
    placed = (P(ROW, "col"),)
    return jax.shard_map(body, mesh=split, in_specs=placed, out_specs=P(ROW, "col"), check_vma=False)
```

```python
import jax
import jax.numpy as jnp
from jax import lax
from jax.sharding import Mesh
from jax.sharding import PartitionSpec as P
from jax.experimental import pallas as pl
from jax.experimental.layout import Layout, with_layout_constraint

ROW = ("chip", "core")


def inner_rows(left, right):
    return lax.dot_general(
        left,
        right,
        (((1,), (1,)), ((), ())),
        precision=lax.Precision.HIGH,
        preferred_element_type=jnp.float32,
    )


def _copy_blocks(block_ref, out_ref):
    per_step, _, width = out_ref.shape
    for t in range(per_step):
        out_ref[t] = block_ref[:, t * width : (t + 1) * width]


def column_chunks(adjacency, n_chunks):
    rows, cols = adjacency.shape
    piece = cols // n_chunks
    per_step = 4 if n_chunks % 4 == 0 else 1
    return pl.pallas_call(
        _copy_blocks,
        grid=(n_chunks // per_step,),
        in_specs=[pl.BlockSpec((rows, piece * per_step), lambda d: (0, d))],
        out_specs=pl.BlockSpec((per_step, rows, piece), lambda d: (d, 0, 0)),
        out_shape=jax.ShapeDtypeStruct((n_chunks, rows, piece), adjacency.dtype),
    )(adjacency)


def col_reduce_scatter(part):
    n_col = lax.axis_size("col")
    me = lax.axis_index("col")
    rows, cols = part.shape
    width = cols // n_col
    blocks = part.reshape(rows, n_col, width)
    total = lax.dynamic_index_in_dim(blocks, me, 1, keepdims=False)
    for s in range(1, n_col):
        send = lax.dynamic_index_in_dim(blocks, (me + s) % n_col, 1, keepdims=False)
        perm = [(i, (i + s) % n_col) for i in range(n_col)]
        total = total + lax.ppermute(send, "col", perm)
    return total


def row_reduce_scatter(gram, core_major):
    n_chip = lax.axis_size("chip")
    n_core = lax.axis_size("core")
    me = lax.axis_index("core")
    rows, width = gram.shape
    strip = rows // (n_chip * n_core)
    if core_major:
        paired, axis = gram.reshape(n_core, n_chip, strip, width), 0
    else:
        paired, axis = gram.reshape(n_chip, n_core, strip, width), 1
    on_chip = lax.dynamic_index_in_dim(paired, me, axis, keepdims=False)
    for s in range(1, n_core):
        send = lax.dynamic_index_in_dim(paired, (me + s) % n_core, axis, keepdims=False)
        perm = [(i, (i + s) % n_core) for i in range(n_core)]
        on_chip = on_chip + lax.ppermute(send, "core", perm)
    blocks = on_chip
    mine = lax.axis_index("chip")
    total = lax.dynamic_index_in_dim(blocks, mine, 0, keepdims=False)
    for s in range(1, n_chip):
        if n_chip & (n_chip - 1) == 0:
            peer, perm = mine ^ s, [(i, i ^ s) for i in range(n_chip)]
        else:
            peer, perm = (mine + s) % n_chip, [(i, (i + s) % n_chip) for i in range(n_chip)]
        send = lax.dynamic_index_in_dim(blocks, peer, 0, keepdims=False)
        total = total + lax.ppermute(send, "chip", perm)
    return total


def chip_reduce_scatter(on_chip):
    n_chip = lax.axis_size("chip")
    rows, width = on_chip.shape
    blocks = on_chip.reshape(n_chip, rows // n_chip, width)
    mine = lax.axis_index("chip")
    total = lax.dynamic_index_in_dim(blocks, mine, 0, keepdims=False)
    for s in range(1, n_chip):
        if n_chip & (n_chip - 1) == 0:
            peer, perm = mine ^ s, [(i, i ^ s) for i in range(n_chip)]
        else:
            peer, perm = (mine + s) % n_chip, [(i, (i + s) % n_chip) for i in range(n_chip)]
        send = lax.dynamic_index_in_dim(blocks, peer, 0, keepdims=False)
        total = total + lax.ppermute(send, "chip", perm)
    return total


def body(adjacency):
    strip_rows, cols = adjacency.shape
    n_row = lax.axis_size(ROW)
    n_col = lax.axis_size("col")
    n_core = lax.axis_size("core")
    window = strip_rows * n_row // n_col
    piece = cols // n_row
    core_major = n_col == lax.axis_size("chip") and window == n_core * strip_rows
    chunks = column_chunks(adjacency, n_row)
    order = ("core", "chip") if core_major else ROW
    pieces = lax.all_to_all(chunks, order, split_axis=0, concat_axis=0, tiled=True)
    pieces = with_layout_constraint(pieces, Layout((0, 1, 2)))
    own_degree = lax.psum(jnp.sum(adjacency, axis=1), "col")
    if core_major:
        chip_degree = lax.all_gather(own_degree, "core", axis=0, tiled=True)
        pieces, own_degree, chip_degree = lax.optimization_barrier((pieces, own_degree, chip_degree))
        n = n_col
        col_degree = lax.ppermute(chip_degree, ("chip", "col"), [(a * n + b, b * n + a) for a in range(n) for b in range(n)])
    else:
        all_degree = lax.all_gather(own_degree, ROW, axis=0, tiled=True)
        col_degree = lax.dynamic_slice_in_dim(all_degree, lax.axis_index("col") * window, window, 0)
        pieces, own_degree, col_degree = lax.optimization_barrier((pieces, own_degree, col_degree))
    outs = []
    if core_major:
        groups = n_core
        flat = pieces.reshape(n_row * strip_rows, piece)
        by_core = pieces.reshape(n_core, n_col * strip_rows, piece)
        me = lax.axis_index("core")
        for g in range(groups):
            right = by_core[g]
            on_chip = None
            for s in range(1, n_core):
                left = lax.dynamic_index_in_dim(by_core, (me + s) % n_core, 0, keepdims=False)
                perm = [(i, (i + s) % n_core) for i in range(n_core)]
                got = lax.ppermute(inner_rows(left, right), "core", perm)
                on_chip = got if on_chip is None else on_chip + got
            left = lax.dynamic_index_in_dim(by_core, me, 0, keepdims=False)
            on_chip = inner_rows(left, right) + on_chip
            outs.append(col_reduce_scatter(chip_reduce_scatter(on_chip)))
    else:
        groups = 2 if window % 256 == 0 else 1
        sub = window // groups
        flat = pieces.reshape(n_row * strip_rows, piece)
        by_group = flat.reshape(n_col, groups, sub, piece)
        for g in range(groups):
            right = by_group[:, g].reshape(n_col * sub, piece)
            outs.append(col_reduce_scatter(row_reduce_scatter(inner_rows(flat, right), False)))
    shared_sum = jnp.stack(outs, axis=1).reshape(strip_rows, window)
    linked = adjacency[:, :window]
    smaller = jnp.minimum(own_degree[:, None], col_degree[None, :])
    return (shared_sum + linked) / (smaller + 1.0 - linked)


def solution(mesh):
    n_row, n_col = mesh.devices.shape
    split = Mesh(mesh.devices.reshape(n_row // 2, 2, n_col), ("chip", "core", "col"))
    placed = (P(ROW, "col"),)
    return jax.shard_map(body, mesh=split, in_specs=placed, out_specs=P(ROW, "col"), check_vma=False)
```

```python
import jax
import jax.numpy as jnp
from jax import lax
from jax.sharding import Mesh
from jax.sharding import PartitionSpec as P
from jax.experimental import pallas as pl
from jax.experimental.layout import Layout, with_layout_constraint

ROW = ("chip", "core")


def inner_rows(left, right):
    return lax.dot_general(
        left,
        right,
        (((1,), (1,)), ((), ())),
        precision=lax.Precision.HIGH,
        preferred_element_type=jnp.float32,
    )


def _copy_blocks(block_ref, out_ref):
    per_step, _, width = out_ref.shape
    for t in range(per_step):
        out_ref[t] = block_ref[:, t * width : (t + 1) * width]


def column_chunks(adjacency, n_chunks):
    rows, cols = adjacency.shape
    piece = cols // n_chunks
    per_step = 4 if n_chunks % 4 == 0 else 1
    return pl.pallas_call(
        _copy_blocks,
        grid=(n_chunks // per_step,),
        in_specs=[pl.BlockSpec((rows, piece * per_step), lambda d: (0, d))],
        out_specs=pl.BlockSpec((per_step, rows, piece), lambda d: (d, 0, 0)),
        out_shape=jax.ShapeDtypeStruct((n_chunks, rows, piece), adjacency.dtype),
    )(adjacency)


def col_reduce_scatter(part):
    n_col = lax.axis_size("col")
    me = lax.axis_index("col")
    rows, cols = part.shape
    width = cols // n_col
    blocks = part.reshape(rows, n_col, width)
    total = lax.dynamic_index_in_dim(blocks, me, 1, keepdims=False)
    for s in range(1, n_col):
        send = lax.dynamic_index_in_dim(blocks, (me + s) % n_col, 1, keepdims=False)
        perm = [(i, (i + s) % n_col) for i in range(n_col)]
        total = total + lax.ppermute(send, "col", perm)
    return total


def row_reduce_scatter(gram, core_major):
    n_chip = lax.axis_size("chip")
    n_core = lax.axis_size("core")
    me = lax.axis_index("core")
    rows, width = gram.shape
    strip = rows // (n_chip * n_core)
    if core_major:
        paired, axis = gram.reshape(n_core, n_chip, strip, width), 0
    else:
        paired, axis = gram.reshape(n_chip, n_core, strip, width), 1
    on_chip = lax.dynamic_index_in_dim(paired, me, axis, keepdims=False)
    for s in range(1, n_core):
        send = lax.dynamic_index_in_dim(paired, (me + s) % n_core, axis, keepdims=False)
        perm = [(i, (i + s) % n_core) for i in range(n_core)]
        on_chip = on_chip + lax.ppermute(send, "core", perm)
    blocks = on_chip
    mine = lax.axis_index("chip")
    total = lax.dynamic_index_in_dim(blocks, mine, 0, keepdims=False)
    for s in range(1, n_chip):
        if n_chip & (n_chip - 1) == 0:
            peer, perm = mine ^ s, [(i, i ^ s) for i in range(n_chip)]
        else:
            peer, perm = (mine + s) % n_chip, [(i, (i + s) % n_chip) for i in range(n_chip)]
        send = lax.dynamic_index_in_dim(blocks, peer, 0, keepdims=False)
        total = total + lax.ppermute(send, "chip", perm)
    return total


def chip_reduce_scatter(on_chip):
    n_chip = lax.axis_size("chip")
    rows, width = on_chip.shape
    blocks = on_chip.reshape(n_chip, rows // n_chip, width)
    mine = lax.axis_index("chip")
    total = lax.dynamic_index_in_dim(blocks, mine, 0, keepdims=False)
    for s in range(1, n_chip):
        if n_chip & (n_chip - 1) == 0:
            peer, perm = mine ^ s, [(i, i ^ s) for i in range(n_chip)]
        else:
            peer, perm = (mine + s) % n_chip, [(i, (i + s) % n_chip) for i in range(n_chip)]
        send = lax.dynamic_index_in_dim(blocks, peer, 0, keepdims=False)
        total = total + lax.ppermute(send, "chip", perm)
    return total


def body(adjacency):
    strip_rows, cols = adjacency.shape
    n_row = lax.axis_size(ROW)
    n_col = lax.axis_size("col")
    n_core = lax.axis_size("core")
    window = strip_rows * n_row // n_col
    piece = cols // n_row
    core_major = n_col == lax.axis_size("chip") and window == n_core * strip_rows
    chunks = column_chunks(adjacency, n_row)
    order = ("core", "chip") if core_major else ROW
    pieces = lax.all_to_all(chunks, order, split_axis=0, concat_axis=0, tiled=True)
    pieces = with_layout_constraint(pieces, Layout((0, 1, 2)))
    own_degree = lax.psum(jnp.sum(adjacency, axis=1), "col")
    if core_major:
        chip_degree = lax.all_gather(own_degree, "core", axis=0, tiled=True)
        pieces, own_degree, chip_degree = lax.optimization_barrier((pieces, own_degree, chip_degree))
        n = n_col
        col_degree = lax.ppermute(chip_degree, ("chip", "col"), [(a * n + b, b * n + a) for a in range(n) for b in range(n)])
    else:
        all_degree = lax.all_gather(own_degree, ROW, axis=0, tiled=True)
        col_degree = lax.dynamic_slice_in_dim(all_degree, lax.axis_index("col") * window, window, 0)
        pieces, own_degree, col_degree = lax.optimization_barrier((pieces, own_degree, col_degree))
    outs = []
    if core_major:
        groups = n_core
        flat = pieces.reshape(n_row * strip_rows, piece)
        by_core = pieces.reshape(n_core, n_col * strip_rows, piece)
        me = lax.axis_index("core")
        on_chip = None
        for s in range(1, n_core):
            left = lax.dynamic_index_in_dim(by_core, (me + s) % n_core, 0, keepdims=False)
            perm = [(i, (i + s) % n_core) for i in range(n_core)]
            got = lax.ppermute(inner_rows(left, flat), "core", perm)
            on_chip = got if on_chip is None else on_chip + got
        left = lax.dynamic_index_in_dim(by_core, me, 0, keepdims=False)
        on_chip = inner_rows(left, flat) + on_chip
        width = on_chip.shape[1] // groups
        for g in range(groups):
            outs.append(col_reduce_scatter(chip_reduce_scatter(on_chip[:, g * width : (g + 1) * width])))
    else:
        groups = 2 if window % 256 == 0 else 1
        sub = window // groups
        flat = pieces.reshape(n_row * strip_rows, piece)
        by_group = flat.reshape(n_col, groups, sub, piece)
        for g in range(groups):
            right = by_group[:, g].reshape(n_col * sub, piece)
            outs.append(col_reduce_scatter(row_reduce_scatter(inner_rows(flat, right), False)))
    shared_sum = jnp.stack(outs, axis=1).reshape(strip_rows, window)
    linked = adjacency[:, :window]
    smaller = jnp.minimum(own_degree[:, None], col_degree[None, :])
    return (shared_sum + linked) / (smaller + 1.0 - linked)


def solution(mesh):
    n_row, n_col = mesh.devices.shape
    split = Mesh(mesh.devices.reshape(n_row // 2, 2, n_col), ("chip", "core", "col"))
    placed = (P(ROW, "col"),)
    return jax.shard_map(body, mesh=split, in_specs=placed, out_specs=P(ROW, "col"), check_vma=False)
```

```python
import jax
import jax.numpy as jnp
from jax import lax
from jax.sharding import Mesh
from jax.sharding import PartitionSpec as P
from jax.experimental import pallas as pl
from jax.experimental.layout import Layout, with_layout_constraint

ROW = ("chip", "core")


def inner_rows(left, right):
    return lax.dot_general(
        left,
        right,
        (((1,), (1,)), ((), ())),
        precision=lax.Precision.HIGH,
        preferred_element_type=jnp.float32,
    )


def _copy_blocks(block_ref, out_ref):
    per_step, _, width = out_ref.shape
    for t in range(per_step):
        out_ref[t] = block_ref[:, t * width : (t + 1) * width]


def column_chunks(adjacency, n_chunks):
    rows, cols = adjacency.shape
    piece = cols // n_chunks
    per_step = 4 if n_chunks % 4 == 0 else 1
    return pl.pallas_call(
        _copy_blocks,
        grid=(n_chunks // per_step,),
        in_specs=[pl.BlockSpec((rows, piece * per_step), lambda d: (0, d))],
        out_specs=pl.BlockSpec((per_step, rows, piece), lambda d: (d, 0, 0)),
        out_shape=jax.ShapeDtypeStruct((n_chunks, rows, piece), adjacency.dtype),
    )(adjacency)


def col_reduce_scatter(part):
    n_col = lax.axis_size("col")
    me = lax.axis_index("col")
    rows, cols = part.shape
    width = cols // n_col
    blocks = part.reshape(rows, n_col, width)
    total = lax.dynamic_index_in_dim(blocks, me, 1, keepdims=False)
    for s in sorted(range(1, n_col), key=lambda s: -min(s, n_col - s)):
        send = lax.dynamic_index_in_dim(blocks, (me + s) % n_col, 1, keepdims=False)
        perm = [(i, (i + s) % n_col) for i in range(n_col)]
        total = total + lax.ppermute(send, "col", perm)
    return total


def row_reduce_scatter(gram, core_major):
    n_chip = lax.axis_size("chip")
    n_core = lax.axis_size("core")
    me = lax.axis_index("core")
    rows, width = gram.shape
    strip = rows // (n_chip * n_core)
    if core_major:
        paired, axis = gram.reshape(n_core, n_chip, strip, width), 0
    else:
        paired, axis = gram.reshape(n_chip, n_core, strip, width), 1
    on_chip = lax.dynamic_index_in_dim(paired, me, axis, keepdims=False)
    for s in range(1, n_core):
        send = lax.dynamic_index_in_dim(paired, (me + s) % n_core, axis, keepdims=False)
        perm = [(i, (i + s) % n_core) for i in range(n_core)]
        on_chip = on_chip + lax.ppermute(send, "core", perm)
    blocks = on_chip
    mine = lax.axis_index("chip")
    total = lax.dynamic_index_in_dim(blocks, mine, 0, keepdims=False)
    for s in range(1, n_chip):
        if n_chip & (n_chip - 1) == 0:
            peer, perm = mine ^ s, [(i, i ^ s) for i in range(n_chip)]
        else:
            peer, perm = (mine + s) % n_chip, [(i, (i + s) % n_chip) for i in range(n_chip)]
        send = lax.dynamic_index_in_dim(blocks, peer, 0, keepdims=False)
        total = total + lax.ppermute(send, "chip", perm)
    return total


def chip_reduce_scatter(on_chip):
    n_chip = lax.axis_size("chip")
    rows, width = on_chip.shape
    blocks = on_chip.reshape(n_chip, rows // n_chip, width)
    mine = lax.axis_index("chip")
    total = lax.dynamic_index_in_dim(blocks, mine, 0, keepdims=False)
    for s in range(1, n_chip):
        if n_chip & (n_chip - 1) == 0:
            peer, perm = mine ^ s, [(i, i ^ s) for i in range(n_chip)]
        else:
            peer, perm = (mine + s) % n_chip, [(i, (i + s) % n_chip) for i in range(n_chip)]
        send = lax.dynamic_index_in_dim(blocks, peer, 0, keepdims=False)
        total = total + lax.ppermute(send, "chip", perm)
    return total


def body(adjacency):
    strip_rows, cols = adjacency.shape
    n_row = lax.axis_size(ROW)
    n_col = lax.axis_size("col")
    n_core = lax.axis_size("core")
    window = strip_rows * n_row // n_col
    piece = cols // n_row
    core_major = n_col == lax.axis_size("chip") and window == n_core * strip_rows
    chunks = column_chunks(adjacency, n_row)
    order = ("core", "chip") if core_major else ROW
    pieces = lax.all_to_all(chunks, order, split_axis=0, concat_axis=0, tiled=True)
    pieces = with_layout_constraint(pieces, Layout((0, 1, 2)))
    own_degree = lax.psum(jnp.sum(adjacency, axis=1), "col")
    if core_major:
        chip_degree = lax.all_gather(own_degree, "core", axis=0, tiled=True)
        pieces, own_degree, chip_degree = lax.optimization_barrier((pieces, own_degree, chip_degree))
        n = n_col
        col_degree = lax.ppermute(chip_degree, ("chip", "col"), [(a * n + b, b * n + a) for a in range(n) for b in range(n)])
    else:
        all_degree = lax.all_gather(own_degree, ROW, axis=0, tiled=True)
        col_degree = lax.dynamic_slice_in_dim(all_degree, lax.axis_index("col") * window, window, 0)
        pieces, own_degree, col_degree = lax.optimization_barrier((pieces, own_degree, col_degree))
    outs = []
    if core_major:
        groups = n_core
        flat = pieces.reshape(n_row * strip_rows, piece)
        by_core = pieces.reshape(n_core, n_col * strip_rows, piece)
        me = lax.axis_index("core")
        on_chip = None
        for s in range(1, n_core):
            left = lax.dynamic_index_in_dim(by_core, (me + s) % n_core, 0, keepdims=False)
            perm = [(i, (i + s) % n_core) for i in range(n_core)]
            got = lax.ppermute(inner_rows(left, flat), "core", perm)
            on_chip = got if on_chip is None else on_chip + got
        left = lax.dynamic_index_in_dim(by_core, me, 0, keepdims=False)
        on_chip = inner_rows(left, flat) + on_chip
        width = on_chip.shape[1] // groups
        for g in range(groups):
            outs.append(col_reduce_scatter(chip_reduce_scatter(on_chip[:, g * width : (g + 1) * width])))
    else:
        groups = 2 if window % 256 == 0 else 1
        sub = window // groups
        flat = pieces.reshape(n_row * strip_rows, piece)
        by_group = flat.reshape(n_col, groups, sub, piece)
        for g in range(groups):
            right = by_group[:, g].reshape(n_col * sub, piece)
            outs.append(col_reduce_scatter(row_reduce_scatter(inner_rows(flat, right), False)))
    shared_sum = jnp.stack(outs, axis=1).reshape(strip_rows, window)
    linked = adjacency[:, :window]
    smaller = jnp.minimum(own_degree[:, None], col_degree[None, :])
    return (shared_sum + linked) / (smaller + 1.0 - linked)


def solution(mesh):
    n_row, n_col = mesh.devices.shape
    split = Mesh(mesh.devices.reshape(n_row // 2, 2, n_col), ("chip", "core", "col"))
    placed = (P(ROW, "col"),)
    return jax.shard_map(body, mesh=split, in_specs=placed, out_specs=P(ROW, "col"), check_vma=False)
```

```python
import jax
import jax.numpy as jnp
from jax import lax
from jax.sharding import Mesh
from jax.sharding import PartitionSpec as P
from jax.experimental import pallas as pl
from jax.experimental.layout import Layout, with_layout_constraint

ROW = ("chip", "core")


def inner_rows(left, right):
    return lax.dot_general(
        left,
        right,
        (((1,), (1,)), ((), ())),
        precision=lax.Precision.HIGH,
        preferred_element_type=jnp.float32,
    )


def _copy_blocks(block_ref, out_ref):
    per_step, _, width = out_ref.shape
    for t in range(per_step):
        out_ref[t] = block_ref[:, t * width : (t + 1) * width]


def column_chunks(adjacency, n_chunks):
    rows, cols = adjacency.shape
    piece = cols // n_chunks
    per_step = 4 if n_chunks % 4 == 0 else 1
    return pl.pallas_call(
        _copy_blocks,
        grid=(n_chunks // per_step,),
        in_specs=[pl.BlockSpec((rows, piece * per_step), lambda d: (0, d))],
        out_specs=pl.BlockSpec((per_step, rows, piece), lambda d: (d, 0, 0)),
        out_shape=jax.ShapeDtypeStruct((n_chunks, rows, piece), adjacency.dtype),
    )(adjacency)


def col_reduce_scatter(part):
    n_col = lax.axis_size("col")
    me = lax.axis_index("col")
    rows, cols = part.shape
    width = cols // n_col
    blocks = part.reshape(rows, n_col, width)
    total = lax.dynamic_index_in_dim(blocks, me, 1, keepdims=False)
    for s in sorted(range(1, n_col), key=lambda s: -min(s, n_col - s)):
        send = lax.dynamic_index_in_dim(blocks, (me + s) % n_col, 1, keepdims=False)
        perm = [(i, (i + s) % n_col) for i in range(n_col)]
        total = total + lax.ppermute(send, "col", perm)
    return total


def row_reduce_scatter(gram, core_major):
    n_chip = lax.axis_size("chip")
    n_core = lax.axis_size("core")
    me = lax.axis_index("core")
    rows, width = gram.shape
    strip = rows // (n_chip * n_core)
    if core_major:
        paired, axis = gram.reshape(n_core, n_chip, strip, width), 0
    else:
        paired, axis = gram.reshape(n_chip, n_core, strip, width), 1
    on_chip = lax.dynamic_index_in_dim(paired, me, axis, keepdims=False)
    for s in range(1, n_core):
        send = lax.dynamic_index_in_dim(paired, (me + s) % n_core, axis, keepdims=False)
        perm = [(i, (i + s) % n_core) for i in range(n_core)]
        on_chip = on_chip + lax.ppermute(send, "core", perm)
    blocks = on_chip
    mine = lax.axis_index("chip")
    total = lax.dynamic_index_in_dim(blocks, mine, 0, keepdims=False)
    for s in range(1, n_chip):
        if n_chip & (n_chip - 1) == 0:
            peer, perm = mine ^ s, [(i, i ^ s) for i in range(n_chip)]
        else:
            peer, perm = (mine + s) % n_chip, [(i, (i + s) % n_chip) for i in range(n_chip)]
        send = lax.dynamic_index_in_dim(blocks, peer, 0, keepdims=False)
        total = total + lax.ppermute(send, "chip", perm)
    return total


def chip_reduce_scatter(on_chip):
    n_chip = lax.axis_size("chip")
    rows, width = on_chip.shape
    blocks = on_chip.reshape(n_chip, rows // n_chip, width)
    mine = lax.axis_index("chip")
    total = lax.dynamic_index_in_dim(blocks, mine, 0, keepdims=False)
    for s in sorted(range(1, n_chip), key=lambda s: -s):
        if n_chip & (n_chip - 1) == 0:
            peer, perm = mine ^ s, [(i, i ^ s) for i in range(n_chip)]
        else:
            peer, perm = (mine + s) % n_chip, [(i, (i + s) % n_chip) for i in range(n_chip)]
        send = lax.dynamic_index_in_dim(blocks, peer, 0, keepdims=False)
        total = total + lax.ppermute(send, "chip", perm)
    return total


def body(adjacency):
    strip_rows, cols = adjacency.shape
    n_row = lax.axis_size(ROW)
    n_col = lax.axis_size("col")
    n_core = lax.axis_size("core")
    window = strip_rows * n_row // n_col
    piece = cols // n_row
    core_major = n_col == lax.axis_size("chip") and window == n_core * strip_rows
    chunks = column_chunks(adjacency, n_row)
    order = ("core", "chip") if core_major else ROW
    pieces = lax.all_to_all(chunks, order, split_axis=0, concat_axis=0, tiled=True)
    pieces = with_layout_constraint(pieces, Layout((0, 1, 2)))
    own_degree = lax.psum(jnp.sum(adjacency, axis=1), "col")
    if core_major:
        chip_degree = lax.all_gather(own_degree, "core", axis=0, tiled=True)
        pieces, own_degree, chip_degree = lax.optimization_barrier((pieces, own_degree, chip_degree))
        n = n_col
        col_degree = lax.ppermute(chip_degree, ("chip", "col"), [(a * n + b, b * n + a) for a in range(n) for b in range(n)])
    else:
        all_degree = lax.all_gather(own_degree, ROW, axis=0, tiled=True)
        col_degree = lax.dynamic_slice_in_dim(all_degree, lax.axis_index("col") * window, window, 0)
        pieces, own_degree, col_degree = lax.optimization_barrier((pieces, own_degree, col_degree))
    outs = []
    if core_major:
        groups = n_core
        flat = pieces.reshape(n_row * strip_rows, piece)
        by_core = pieces.reshape(n_core, n_col * strip_rows, piece)
        me = lax.axis_index("core")
        on_chip = None
        for s in range(1, n_core):
            left = lax.dynamic_index_in_dim(by_core, (me + s) % n_core, 0, keepdims=False)
            perm = [(i, (i + s) % n_core) for i in range(n_core)]
            got = lax.ppermute(inner_rows(left, flat), "core", perm)
            on_chip = got if on_chip is None else on_chip + got
        left = lax.dynamic_index_in_dim(by_core, me, 0, keepdims=False)
        on_chip = inner_rows(left, flat) + on_chip
        width = on_chip.shape[1] // groups
        for g in range(groups):
            outs.append(col_reduce_scatter(chip_reduce_scatter(on_chip[:, g * width : (g + 1) * width])))
    else:
        groups = 2 if window % 256 == 0 else 1
        sub = window // groups
        flat = pieces.reshape(n_row * strip_rows, piece)
        by_group = flat.reshape(n_col, groups, sub, piece)
        for g in range(groups):
            right = by_group[:, g].reshape(n_col * sub, piece)
            outs.append(col_reduce_scatter(row_reduce_scatter(inner_rows(flat, right), False)))
    shared_sum = jnp.stack(outs, axis=1).reshape(strip_rows, window)
    linked = adjacency[:, :window]
    smaller = jnp.minimum(own_degree[:, None], col_degree[None, :])
    return (shared_sum + linked) / (smaller + 1.0 - linked)


def solution(mesh):
    n_row, n_col = mesh.devices.shape
    split = Mesh(mesh.devices.reshape(n_row // 2, 2, n_col), ("chip", "core", "col"))
    placed = (P(ROW, "col"),)
    return jax.shard_map(body, mesh=split, in_specs=placed, out_specs=P(ROW, "col"), check_vma=False)
```
